32 devices in a mesh: clu: 8 (over z, y), sub: 4 (over x, core).
Axes of the slice: x: 2, y: 2, z: 4, core: 2. Of those that a mesh axis runs over, the one named last changes fastest.
Arguments:
- queries: bfloat16 [32768, 768], P(('clu', 'sub')), may hold values from -6 to 6
- pos_cols: int32 [6, 32768], P(None, 'clu'), may hold values from 0 to 1023, as said below
- label_ids: int32 [8192], P(('clu', 'sub')), may hold values from 0 to 65535, as said below
- slot_of: int32 [65536], replicated, may hold values from 0 to 65535, as said below
- label_table: bfloat16 [768, 65536], P('sub', 'clu'), may hold values from -5 to 5
- label_freq: int32 [65536], P('clu'), may hold values from 1 to 65535
- first_moment: float32 [768, 65536], P('sub', 'clu'), may hold values from -3 to 3
- second_moment: float32 [768, 65536], P('sub', 'clu'), may hold values from 0.05 to 1
Outputs:
- new_table: bfloat16 [768, 65536], P('sub', 'clu')
- new_first: float32 [768, 65536], P('sub', 'clu')
- new_second: float32 [768, 65536], P('sub', 'clu')
- mean_loss: float32 [], replicated
The draws below stay inside these ranges and needn't reach their ends.
Inputs may be any that keep to these rules, and one draw needn't show every extreme that they name: `label_ids`: the 256 ids of one device's list are distinct. Among them at most 96 have slot_of[id] // 8192 equal to one value; in every draw one such value is reached by exactly 96 ids of every list. `pos_cols`: each query names 1 to 6 distinct columns of its batch's 4 * 256 columns; entries of a query may repeat. `slot_of`: A permutation of the label slots.
All inputs are finite; a program needn't handle non-finite values.
Results may differ from the reference program's by a relative error of at most 0.0023.
Values may be sent and summed in bfloat16 or wider, within the bound.
No kernel may reach another device: no remote copies, remote signals or barrier semaphores. Data moves between devices by JAX's collectives and lax.ppermute only.
A program may use at most 128 MiB of HBM per device.

```python
import math
import jax
import jax.numpy as jnp
from jax import lax

D = 768
LAB_DEV = 8192
P_SIZE = 256
Q_DEV = 1024
K = 6
LOSS_SCALE = 1048576
LABELS = 65536
BATCHQ = 4096
QUERIES = 32768
CAP = 96


def shared_perm(key):
    return jax.random.permutation(jax.random.fold_in(key, 7), LABELS).astype(jnp.int32)


def draw_slot_of(key, part):
    return shared_perm(key)


def draw_label_ids(key, part):
    perm = shared_perm(key)
    inverse = jnp.zeros((LABELS,), jnp.int32).at[perm].set(jnp.arange(LABELS, dtype=jnp.int32))
    owners = LABELS // LAB_DEV
    lists = QUERIES // Q_DEV
    hottest = jax.random.randint(jax.random.fold_in(key, 11), (), 0, owners)
    is_hot = jnp.arange(owners, dtype=jnp.int32)[None, :] == hottest
    others = P_SIZE - CAP
    weights = jax.random.randint(jax.random.fold_in(key, 12), (lists, owners), 1, 4)
    weights = jnp.where(is_hot, 0, weights)
    total = jnp.sum(weights, axis=1, keepdims=True)
    counts = weights * others // total
    remain = others - jnp.sum(counts, axis=1, keepdims=True)
    ranking = jax.vmap(lambda k: jax.random.permutation(k, owners))(jax.random.split(jax.random.fold_in(key, 13), lists)).astype(jnp.int32)
    hot_rank = jnp.sum(jnp.where(is_hot, ranking, 0), axis=1, keepdims=True)
    adjusted = ranking - (ranking > hot_rank).astype(jnp.int32)
    counts = counts + jnp.where(jnp.logical_and(jnp.logical_not(is_hot), adjusted < remain), 1, 0)
    counts = jnp.where(is_hot, CAP, counts)
    ends = jnp.cumsum(counts, axis=1)
    starts = ends - counts
    spots = jnp.arange(P_SIZE, dtype=jnp.int32)
    owner_of = jnp.sum((ends[:, None, :] <= spots[None, :, None]).astype(jnp.int32), axis=2)
    within = spots[None, :] - jnp.take_along_axis(starts, owner_of, axis=1)
    offsets = jax.random.randint(jax.random.fold_in(key, 14), (lists, owners), 0, LAB_DEV)
    strides = jax.random.randint(jax.random.fold_in(key, 15), (lists, owners), 1, LAB_DEV // CAP + 1)
    local_row = (jnp.take_along_axis(offsets, owner_of, axis=1) + within * jnp.take_along_axis(strides, owner_of, axis=1)) % LAB_DEV
    slot_ids = owner_of * LAB_DEV + local_row
    shuffle = jax.vmap(lambda k: jax.random.permutation(k, P_SIZE))(jax.random.split(jax.random.fold_in(key, 16), lists)).astype(jnp.int32)
    slot_ids = jnp.take_along_axis(slot_ids, shuffle, axis=1)
    return inverse[slot_ids].reshape(-1).astype(jnp.int32)


def draw_pos_cols(key, part):
    batches = QUERIES // BATCHQ
    columns = BATCHQ // Q_DEV * P_SIZE
    batch_of = jnp.arange(QUERIES, dtype=jnp.int32) // BATCHQ
    ceiling = 1 + (K - 1) * batch_of // max(batches - 1, 1)
    number = 1 + jax.random.randint(jax.random.fold_in(key, 21), (QUERIES,), 0, ceiling)
    anchor = jax.random.randint(jax.random.fold_in(key, 22), (QUERIES,), 0, columns)
    spacing = jax.random.randint(jax.random.fold_in(key, 23), (QUERIES,), 1, columns // K + 1)
    order = jnp.arange(K, dtype=jnp.int32)[:, None]
    listed = (anchor[None, :] + order * spacing[None, :]) % columns
    listed = jnp.where(order < number[None, :], listed, listed[0:1, :])
    return listed.astype(jnp.int32)


def draw_label_freq(key, part):
    power = jax.random.randint(jax.random.fold_in(key, 31), (LABELS,), 0, 16)
    extra = jax.random.randint(jax.random.fold_in(key, 32), (LABELS,), 0, 65536)
    return (jnp.left_shift(jnp.int32(1), power) + jnp.right_shift(extra, 16 - power)).astype(jnp.int32)


def block_levels(own_key, extent, cuts, smallest, high):
    gain, own = 1.0, jax.random.fold_in(own_key, 6)
    for axis_at, shards_of in cuts:
        draws = jnp.exp(jax.random.uniform(jax.random.fold_in(own, axis_at), (shards_of,), jnp.float32, smallest / len(cuts), high / len(cuts)))
        gain = gain * jnp.repeat(draws, extent[axis_at] // shards_of).reshape([-1 if axis == axis_at else 1 for axis in range(len(extent))])
    return gain


def gaussian(own_key, shape, width, limit, pieces=(), kind=jnp.bfloat16):
    level = block_levels(own_key, shape, pieces, -0.22, 0.18) if pieces else 1.0
    result = jax.random.normal(own_key, shape, jnp.float32) * width * level
    return jnp.minimum(jnp.maximum(result, -limit), limit).astype(kind)


def setup_inputs(seed: int = 0) -> dict:
    key_of = jax.random.split(jax.random.key(seed), 9)
    return {
        "queries": gaussian(key_of[0], (QUERIES, D), 1.0, 6.0, ((0, 32),)),
        "pos_cols": draw_pos_cols(jax.random.fold_in(key_of[8], 71), 0),
        "label_ids": draw_label_ids(jax.random.fold_in(key_of[8], 71), 0),
        "slot_of": draw_slot_of(jax.random.fold_in(key_of[8], 71), 0),
        "label_table": gaussian(key_of[4], (D, LABELS), 1.0, 5.0, ((0, 4), (1, 8))),
        "label_freq": draw_label_freq(jax.random.fold_in(key_of[8], 71), 0),
        "first_moment": gaussian(key_of[6], (D, LABELS), 0.5, 3.0, ((0, 4), (1, 8)), jnp.float32),
        "second_moment": jnp.clip(jnp.exp(math.log(1.0) - 2.9957323 * jax.random.uniform(key_of[7], (D, LABELS), jnp.float32) ** block_levels(key_of[7], (D, LABELS), ((0, 4), (1, 8)), -0.2, 0.2)), 0.05, 1.0),
    }


FOCUS_ALPHA = 0.25
BETA_FIRST = 0.9
BETA_SECOND = 0.999
LEARN_RATE = 0.01
EPSILON = 1e-08

def focal_terms(logits, target, weight):
    probability = jax.nn.sigmoid(logits)
    complement = 1.0 - probability
    soft_neg = jax.nn.softplus(-logits)
    soft_pos = jax.nn.softplus(logits)
    weight_row = weight[None, :]
    losses = weight_row * (target * FOCUS_ALPHA * complement * complement * soft_neg + (1.0 - target) * (1.0 - FOCUS_ALPHA) * probability * probability * soft_pos)
    slopes = weight_row * (target * -FOCUS_ALPHA * complement * complement * (2.0 * probability * soft_neg + complement) + (1.0 - target) * (1.0 - FOCUS_ALPHA) * probability * probability * (2.0 * complement * soft_pos + probability))
    return (losses, slopes.astype(jnp.bfloat16))

def positive_mask(listed, columns):
    found = jnp.zeros((listed.shape[1], columns.shape[0]), jnp.float32)
    for k in range(listed.shape[0]):
        found = jnp.maximum(found, (listed[k][:, None] == columns[None, :]).astype(jnp.float32))
    return found

def reference(queries, pos_cols, label_ids, slot_of, label_table, label_freq, first_moment, second_moment):
    table_rows = label_table.T
    first_rows = first_moment.T
    second_rows = second_moment.T
    group = BATCHQ // Q_DEV
    lists = label_ids.shape[0] // P_SIZE
    slot_ids = slot_of[label_ids]
    fetched = table_rows[slot_ids].reshape(lists, P_SIZE, D)
    weights = (1.0 / (1.0 + jnp.log1p(label_freq[slot_ids].astype(jnp.float32)))).reshape(lists, P_SIZE)
    inv_root = 1.0 / math.sqrt(D)

    def one_list(which):
        batch = which // group
        member = which % group
        batch_q = lax.dynamic_slice_in_dim(queries, batch * BATCHQ, BATCHQ, 0)
        batch_pos = lax.dynamic_slice_in_dim(pos_cols, batch * BATCHQ, BATCHQ, 1)
        columns = member * P_SIZE + jnp.arange(P_SIZE, dtype=jnp.int32)
        target = positive_mask(batch_pos, columns)
        logits = jnp.dot(batch_q, fetched[which].T, preferred_element_type=jnp.float32) * inv_root
        losses, slopes = focal_terms(logits, target, weights[which])
        gradient = jnp.dot(slopes.T, batch_q, preferred_element_type=jnp.float32)
        return (gradient, jnp.sum(losses), jnp.sum(target))
    grads, loss_parts, counts = lax.map(one_list, jnp.arange(lists, dtype=jnp.int32))
    positives = jnp.sum(counts)
    factor = LOSS_SCALE / (math.sqrt(D) * positives)
    scaled = (grads * factor).reshape(lists * P_SIZE, D)
    summed = jnp.zeros((LABELS, D), jnp.float32).at[slot_ids].add(scaled)
    hits = jnp.zeros((LABELS,), jnp.float32).at[slot_ids].add(1.0) > 0.5
    new_first = jnp.where(hits[:, None], BETA_FIRST * first_rows + (1.0 - BETA_FIRST) * summed, first_rows)
    new_second = jnp.where(hits[:, None], BETA_SECOND * second_rows + (1.0 - BETA_SECOND) * summed * summed, second_rows)
    base_table = table_rows.astype(jnp.float32)
    moved = base_table - LEARN_RATE * new_first / (jnp.sqrt(new_second) + EPSILON)
    new_table = jnp.where(hits[:, None], moved, base_table).astype(jnp.bfloat16)
    mean_loss = jnp.sum(loss_parts) / positives
    return (new_table.T, new_first.T, new_second.T, mean_loss)
```

```python
import math

import jax
import jax.numpy as jnp
from jax import lax
from jax.experimental import pallas as pl
from jax.sharding import PartitionSpec as P

LOSS_SCALE = 1048576


FOCUS_ALPHA = 0.25
BETA_FIRST = 0.9
BETA_SECOND = 0.999
LEARN_RATE = 0.01
EPSILON = 1e-08


def focal_terms(logits, target, weight):
    probability = jax.nn.sigmoid(logits)
    complement = 1.0 - probability
    soft_neg = jax.nn.softplus(-logits)
    soft_pos = jax.nn.softplus(logits)
    weight_row = weight[None, :]
    losses = weight_row * (
        target * FOCUS_ALPHA * complement * complement * soft_neg
        + (1.0 - target) * (1.0 - FOCUS_ALPHA) * probability * probability * soft_pos
    )
    slopes = weight_row * (
        target
        * -FOCUS_ALPHA
        * complement
        * complement
        * (2.0 * probability * soft_neg + complement)
        + (1.0 - target)
        * (1.0 - FOCUS_ALPHA)
        * probability
        * probability
        * (2.0 * complement * soft_pos + probability)
    )
    return (losses, slopes.astype(jnp.bfloat16))


def positive_mask(listed, columns):
    found = jnp.zeros((listed.shape[1], columns.shape[0]), jnp.float32)
    for k in range(listed.shape[0]):
        found = jnp.maximum(found, (listed[k][:, None] == columns[None, :]).astype(jnp.float32))
    return found


def adam_kernel(table_ref, first_ref, second_ref, rows_ref, table_out, first_out, second_out):
    col_width = table_ref.shape[0]
    flipped = jnp.transpose(rows_ref[...], (1, 0))
    grad = flipped[:col_width, :]
    hits = flipped[col_width : col_width + 1, :] > 0.5
    first = first_ref[...]
    second = second_ref[...]
    new_first = jnp.where(hits, BETA_FIRST * first + (1.0 - BETA_FIRST) * grad, first)
    new_second = jnp.where(
        hits, BETA_SECOND * second + (1.0 - BETA_SECOND) * grad * grad, second
    )
    base_table = table_ref[...].astype(jnp.float32)
    moved = base_table - LEARN_RATE * new_first / (jnp.sqrt(new_second) + EPSILON)
    table_out[...] = jnp.where(hits, moved, base_table).astype(jnp.bfloat16)
    first_out[...] = new_first
    second_out[...] = new_second


def adam_update(label_table, first_moment, second_moment, summed_rows):
    col_width, lab_rows = label_table.shape
    pad_width = summed_rows.shape[1]
    tile = 512
    spec = pl.BlockSpec((col_width, tile), lambda j: (0, j))
    return pl.pallas_call(
        adam_kernel,
        grid=(lab_rows // tile,),
        in_specs=[spec, spec, spec, pl.BlockSpec((tile, pad_width), lambda j: (j, 0))],
        out_specs=[spec, spec, spec],
        out_shape=[
            jax.ShapeDtypeStruct(label_table.shape, jnp.bfloat16),
            jax.ShapeDtypeStruct(first_moment.shape, jnp.float32),
            jax.ShapeDtypeStruct(second_moment.shape, jnp.float32),
        ],
    )(label_table, first_moment, second_moment, summed_rows)


def body(
    queries, pos_cols, label_ids, slot_of, label_table, label_freq, first_moment, second_moment
):
    clu_count = lax.axis_size("clu")
    sub_count = lax.axis_size("sub")
    my_sub = lax.axis_index("sub")
    n_dev = clu_count * sub_count
    list_len = label_ids.shape[0]
    col_width = label_table.shape[0]
    lab_rows = label_table.shape[1]
    width = col_width * sub_count
    slot_cap = 3 * list_len // clu_count
    inv_root = 1.0 / math.sqrt(width)
    axes = ("clu", "sub")

    slot_ids = slot_of[label_ids]
    owner_of = slot_ids // lab_rows
    local_row = slot_ids % lab_rows
    one_hot = (owner_of[:, None] == jnp.arange(clu_count, dtype=jnp.int32)[None, :]).astype(
        jnp.int32
    )
    slot_rank = jnp.sum(jnp.cumsum(one_hot, axis=0) * one_hot, axis=1) - 1
    key = owner_of * slot_cap + slot_rank
    match = key[:, None] == jnp.arange(clu_count * slot_cap, dtype=jnp.int32)[None, :]
    requests = jnp.max(jnp.where(match, local_row[:, None], -1), axis=0)
    requests = jnp.where(requests < 0, lab_rows, requests)
    inverse = jnp.max(jnp.where(match, jnp.arange(list_len, dtype=jnp.int32)[:, None], -1), axis=0)
    inverse = jnp.where(inverse < 0, list_len, inverse)

    columns = my_sub * list_len + jnp.arange(list_len, dtype=jnp.int32)
    lower = my_sub * list_len
    fresh_total = jnp.zeros((), jnp.int32)
    for k in range(pos_cols.shape[0]):
        fresh = jnp.logical_and(pos_cols[k] >= lower, pos_cols[k] < lower + list_len)
        for j in range(k):
            fresh = jnp.logical_and(fresh, pos_cols[j] != pos_cols[k])
        fresh_total = fresh_total + jnp.sum(fresh.astype(jnp.int32))

    wanted = jnp.broadcast_to(
        requests.reshape(clu_count, 1, slot_cap), (clu_count, sub_count, slot_cap)
    ).reshape(n_dev, slot_cap)
    wanted = jnp.concatenate(
        [wanted, jnp.broadcast_to(fresh_total, (n_dev, 1)).astype(jnp.int32)], axis=1
    )
    asked_all = lax.all_to_all(wanted, axes, split_axis=0, concat_axis=0, tiled=True)
    positives = jnp.sum(asked_all[:, slot_cap]).astype(jnp.float32)
    asked = asked_all[:, :slot_cap]
    factor = LOSS_SCALE / (math.sqrt(width) * positives)

    picked = jnp.clip(asked, 0, lab_rows - 1).reshape(-1)
    table_rows = label_table.T
    sent_rows = table_rows[picked].reshape(n_dev, slot_cap, col_width)
    got = lax.all_to_all(sent_rows, axes, split_axis=0, concat_axis=0, tiled=True)
    got = got.reshape(clu_count, sub_count, slot_cap, col_width)
    fetched = got[owner_of, :, slot_rank, :].reshape(list_len, width)

    all_freq = lax.all_gather(label_freq, "clu", axis=0, tiled=True)
    fetched_freq = all_freq[slot_ids]
    weights = 1.0 / (1.0 + jnp.log1p(fetched_freq.astype(jnp.float32)))

    initial = (jnp.zeros((list_len, width), jnp.float32), jnp.zeros((), jnp.float32))
    arrived = lax.all_gather(queries, "sub", axis=0, tiled=True)
    count_rows = arrived.shape[0]
    block = 512

    def one_block(step, partial_value):
        q_block = lax.dynamic_slice_in_dim(arrived, step * block, block, 0)
        p_block = lax.dynamic_slice_in_dim(pos_cols, step * block, block, 1)
        target = positive_mask(p_block, columns)
        logits = (
            lax.dot_general(
                q_block, fetched, (((1,), (1,)), ((), ())), preferred_element_type=jnp.float32
            )
            * inv_root
        )
        losses, slopes = focal_terms(logits, target, weights)
        gradient = partial_value[0] + lax.dot_general(
            slopes, q_block, (((0,), (0,)), ((), ())), preferred_element_type=jnp.float32
        )
        return (gradient, partial_value[1] + jnp.sum(losses))

    gradient, loss_here = lax.fori_loop(0, count_rows // block, one_block, initial)
    outgoing = gradient * factor
    padded = jnp.concatenate([outgoing, jnp.zeros((1, width), jnp.float32)], axis=0)
    buffer = padded[inverse].reshape(clu_count, slot_cap, sub_count, col_width)
    buffer = jnp.transpose(buffer, (0, 2, 1, 3)).reshape(n_dev, slot_cap, col_width)
    loss_row = jnp.zeros((n_dev, 1, col_width), jnp.float32).at[:, 0, 0].set(loss_here)
    buffer = jnp.concatenate([buffer, loss_row], axis=1)
    received = lax.all_to_all(buffer, axes, split_axis=0, concat_axis=0, tiled=True)
    loss_sum = jnp.sum(received[:, slot_cap, 0])
    incoming = received[:, :slot_cap, :].reshape(n_dev * slot_cap, col_width)
    pad_width = 256 * ((col_width + 1 + 255) // 256)
    incoming = jnp.concatenate(
        [
            incoming,
            jnp.ones((n_dev * slot_cap, 1), jnp.float32),
            jnp.zeros((n_dev * slot_cap, pad_width - col_width - 1), jnp.float32),
        ],
        axis=1,
    )
    owner_requests = asked.reshape(-1)
    summed_rows = (
        jnp.zeros((lab_rows + 1, pad_width), jnp.float32).at[owner_requests].add(incoming)
    )
    new_table, new_first, new_second = adam_update(
        label_table, first_moment, second_moment, summed_rows
    )
    mean_loss = loss_sum / positives
    return (new_table, new_first, new_second, mean_loss)


def solution(mesh):
    in_specs = (
        P(("clu", "sub"), None),
        P(None, "clu"),
        P(("clu", "sub")),
        P(),
        P("sub", "clu"),
        P("clu"),
        P("sub", "clu"),
        P("sub", "clu"),
    )
    out_specs = (P("sub", "clu"), P("sub", "clu"), P("sub", "clu"), P())
    return jax.shard_map(body, mesh=mesh, in_specs=in_specs, out_specs=out_specs, check_vma=False)
```
